32 devices in a mesh: pair: 8 (over z, y), virt: 4 (over x, core).
Axes of the slice: x: 2, y: 2, z: 4, core: 2. Of those that a mesh axis runs over, the one named last changes fastest.
Arguments:
- amps_pm: bfloat16 [64, 64, 4096], P(('pair', 'virt')), may hold values from -6 to 6
- integrals: bfloat16 [32, 4096, 2048], P(('pair', 'virt')), may hold values from -0.046875 to 0.046875
- fock_vv: bfloat16 [512, 512], replicated, may hold values from -0.25 to 0.25
- blk_tiles: int32 [32, 2], replicated, may hold values from 0 to 63, as said below
- blk_mask: int32 [32], replicated, may hold values 0 or 1
Outputs:
- sigma: bfloat16 [64, 64, 2048], P('pair', 'virt')
The draws below stay inside these ranges and needn't reach their ends.
Inputs may be any that keep to these rules, and one draw needn't show every extreme that they name: Each row is (input tile pair, output tile pair). Integral tile r belongs to device r // 1 of the joined axis pair+virt, and its input tile pair lies in that device's virt slab: blk_tiles[r, 0] // 16 == (r) % 4. No two rows are equal.
All inputs are finite; a program needn't handle non-finite values.
Results may differ from the reference program's by a relative error of at most 0.0033.
Values may be sent and summed in bfloat16 or wider, within the bound.
No kernel may reach another device: no remote copies, remote signals or barrier semaphores. Data moves between devices by JAX's collectives and lax.ppermute only.
A program may use at most 128 MiB of HBM per device.

```python
import jax
import jax.numpy as jnp
from jax import lax

TILE = 64
NVT = 8
A_W = 8
AS = 32
BLK_DEV = 1
NV = 512
NT = 64
TP_DEV = 16
TT = 4096
OC = 2048
PAIRS = 64
NBLK = 32
N_PAIR = 8
N_VIRT = 4


def draw_blk_tiles(key, part):
    total_codes = TP_DEV * NT
    picked = N_PAIR * BLK_DEV
    key_list = jax.random.split(jax.random.fold_in(key, 11), N_VIRT)
    order_keys = jax.random.split(jax.random.fold_in(key, 23), N_VIRT)

    def one_column(one_key, order_key):
        inner = 1 + jax.random.permutation(one_key, total_codes - 2)
        ends = jnp.array([0, total_codes - 1], dtype=jnp.int32)
        listed = jnp.concatenate([ends, inner.astype(jnp.int32)])[:picked]
        return listed[jax.random.permutation(order_key, picked)]
    combos = jax.vmap(one_column)(key_list, order_keys)
    chosen = combos.reshape(N_VIRT, N_PAIR, BLK_DEV)
    chosen = jnp.transpose(chosen, (1, 0, 2))
    slab_start = (jnp.arange(N_VIRT, dtype=jnp.int32) * TP_DEV)[None, :, None]
    tile_in = slab_start + chosen // NT
    tile_out = chosen % NT
    return jnp.stack([tile_in, tile_out], axis=-1).reshape(NBLK, 2).astype(jnp.int32)


def touch_ends(values, key, least, largest):
    place = [jax.random.randint(jax.random.fold_in(key, axis), (), 0, length) for axis, length in enumerate(values.shape)]
    widest = values.shape.index(max(values.shape))
    next_to = place[:widest] + [(place[widest] + 1) % values.shape[widest]] + place[widest + 1:]
    return values.at[tuple(place)].set(least).at[tuple(next_to)].set(largest)


def block_levels(own_key, dims, cuts, least, top_value):
    gain, own = 1.0, jax.random.fold_in(own_key, 6)
    for dim, shards_of in cuts:
        steps = jnp.exp(jax.random.uniform(jax.random.fold_in(own, dim), (shards_of,), jnp.float32, least / len(cuts), top_value / len(cuts)))
        gain = gain * jnp.repeat(steps, dims[dim] // shards_of).reshape([-1 if axis == dim else 1 for axis in range(len(dims))])
    return gain


def noise(stream_key, shape, deviation, bound, shards=(), held_as=jnp.bfloat16):
    entries = jax.random.normal(stream_key, shape, jnp.float32) * deviation
    if len(shards) > 0:
        entries = block_levels(stream_key, shape, shards, -0.22, 0.18) * entries
    return jnp.clip(entries, min=-bound, max=bound).astype(held_as)


def setup_inputs(seed: int = 0) -> dict:
    arg_keys = jax.random.split(jax.random.key(seed), 6)
    amps_pm = noise(arg_keys[0], (PAIRS, NT, TT), 1.0, 6.0, ((0, 32),))
    integrals = noise(arg_keys[1], (NBLK, TT, OC), (4 * TT) ** -0.5, 0.046875, ((0, 32),))
    fock_vv = noise(arg_keys[2], (NV, NV), NV ** -0.5, 0.25)
    blk_tiles = draw_blk_tiles(jax.random.fold_in(arg_keys[5], 71), 0)
    blk_mask = touch_ends((jax.random.randint(arg_keys[4], (NBLK,), 0, 4) < 3).astype(jnp.int32), jax.random.fold_in(arg_keys[4], 1), 0, 1)
    return dict(amps_pm=amps_pm, integrals=integrals, fock_vv=fock_vv, blk_tiles=blk_tiles, blk_mask=blk_mask)


def reference(amps_pm, integrals, fock_vv, blk_tiles, blk_mask):
    pair_count, n_tiles, tile_len = amps_pm.shape
    out_cols = integrals.shape[2]

    def add_block(running, inputs):
        one_block, tile_pair, keep_flag = inputs
        source = lax.dynamic_index_in_dim(amps_pm, tile_pair[0], 1, keepdims=False)
        product = jnp.dot(source, one_block, preferred_element_type=jnp.float32)
        product = product * keep_flag.astype(jnp.float32)
        current = lax.dynamic_index_in_dim(running, tile_pair[1], 1, keepdims=False)
        return lax.dynamic_update_index_in_dim(running, current + product, tile_pair[1], 1), None

    start_sum = jnp.zeros((pair_count, n_tiles, out_cols), jnp.float32)
    ladder, _ = lax.scan(add_block, start_sum, (integrals, blk_tiles, blk_mask))
    sub_rows = amps_pm[:, :, :out_cols].astype(jnp.float32).reshape(pair_count, A_W, NVT, AS, TILE)
    fock_four = fock_vv.astype(jnp.float32).reshape(NVT, TILE, NVT, TILE)
    onebody = jnp.einsum('pkqsd,bjqd->pkbsj', sub_rows, fock_four).reshape(pair_count, n_tiles, out_cols)
    return (ladder + onebody).astype(jnp.bfloat16)
```

```python
import jax
import jax.numpy as jnp
from jax import lax
from jax.sharding import PartitionSpec as P

TILE = 64
NVT = 8
AS = 32


def per_device(amps_pm, integrals, fock_vv, blk_tiles, blk_mask):
    n_virt = lax.axis_size("virt")
    n_pair = lax.axis_size("pair")
    n_dev = n_virt * n_pair
    pm_rows, n_tiles, tile_len = amps_pm.shape
    out_cols = integrals.shape[2]
    slab = n_tiles // n_virt
    device = lax.axis_index(("pair", "virt"))
    virt_idx = lax.axis_index("virt")
    p_grp = pm_rows * n_virt

    tin_all = blk_tiles[:, 0]
    picked = jnp.take(amps_pm, tin_all, axis=1)
    picked = jnp.transpose(picked, (1, 0, 2))
    chosen = lax.all_to_all(picked, ("pair", "virt"), 0, 0, tiled=True)
    chosen = chosen.reshape(n_dev * pm_rows, tile_len)

    sub = lax.all_to_all(
        amps_pm[:, :, :out_cols], "virt", split_axis=1, concat_axis=0, tiled=True
    )
    sub = sub.reshape(p_grp, slab // NVT, NVT, AS, TILE)
    fock_four = fock_vv.reshape(NVT, TILE, NVT, TILE)
    onebody = jnp.einsum(
        "pkqsd,bjqd->pkbsj", sub, fock_four, preferred_element_type=jnp.float32
    ).reshape(p_grp, slab, out_cols)

    own_tiles = lax.dynamic_index_in_dim(blk_tiles, device, 0, keepdims=False)
    own_mask = lax.dynamic_index_in_dim(blk_mask, device, 0, keepdims=False)
    product = jnp.dot(chosen, integrals[0], preferred_element_type=jnp.float32)
    product = (product * own_mask.astype(jnp.float32)).astype(jnp.bfloat16)

    dest_virt = own_tiles[1] // slab
    select = (jnp.arange(n_virt, dtype=jnp.int32) == dest_virt).astype(jnp.bfloat16)
    outgoing = product.reshape(n_pair, 1, p_grp, out_cols) * select[None, :, None, None]
    outgoing = outgoing.reshape(n_dev, p_grp, out_cols)
    received = lax.all_to_all(outgoing, ("pair", "virt"), 0, 0, tiled=True)

    my_tiles = virt_idx * slab + jnp.arange(slab, dtype=jnp.int32)
    one_hot = (blk_tiles[:, 1][:, None] == my_tiles[None, :]).astype(jnp.bfloat16)
    ladder = jnp.einsum(
        "rpo,rt->pto", received, one_hot, preferred_element_type=jnp.float32
    )
    return (ladder + onebody).astype(jnp.bfloat16)


def solution(mesh):
    return jax.shard_map(
        per_device,
        mesh=mesh,
        in_specs=(P(("pair", "virt"), None, None), P(("pair", "virt"), None, None), P(), P(), P()),
        out_specs=P("pair", "virt", None),
        check_vma=False,
    )
```

```python
import jax
import jax.numpy as jnp
from jax import lax
from jax.sharding import PartitionSpec as P

TILE = 64
NVT = 8
AS = 32
N_CHUNK = 2


def per_device(amps_pm, integrals, fock_vv, blk_tiles, blk_mask):
    n_virt = lax.axis_size("virt")
    n_pair = lax.axis_size("pair")
    n_dev = n_virt * n_pair
    pm_rows, n_tiles, tile_len = amps_pm.shape
    out_cols = integrals.shape[2]
    slab = n_tiles // n_virt
    device = lax.axis_index(("pair", "virt"))
    virt_idx = lax.axis_index("virt")
    p_grp = pm_rows * n_virt

    tin_all = blk_tiles[:, 0]
    picked = jnp.take(amps_pm, tin_all, axis=1)
    picked = jnp.transpose(picked, (1, 0, 2))
    chosen = lax.all_to_all(picked, ("pair", "virt"), 0, 0, tiled=True)
    chosen = chosen.reshape(n_dev * pm_rows, tile_len)

    sub = lax.all_to_all(
        amps_pm[:, :, :out_cols], "virt", split_axis=1, concat_axis=0, tiled=True
    )
    sub = sub.reshape(p_grp, slab // NVT, NVT, AS, TILE)
    fock_four = fock_vv.reshape(NVT, TILE, NVT, TILE)
    onebody = jnp.einsum(
        "pkqsd,bjqd->pkbsj", sub, fock_four, preferred_element_type=jnp.float32
    ).reshape(p_grp, slab, out_cols)

    own_mask = lax.dynamic_index_in_dim(blk_mask, device, 0, keepdims=False)
    own_mask = own_mask.astype(jnp.float32)

    tout = blk_tiles[:, 1].reshape(n_pair, n_virt)
    my_tiles = virt_idx * slab + jnp.arange(slab, dtype=jnp.int32)
    bits = []
    b = n_virt // 2
    while b >= 1:
        bits.append(b)
        b //= 2

    width = out_cols // N_CHUNK
    pieces = []
    for c in range(N_CHUNK):
        cols = integrals[0, :, c * width:(c + 1) * width]
        product = jnp.dot(chosen, cols, preferred_element_type=jnp.float32)
        product = (product * own_mask).astype(jnp.bfloat16)
        held = lax.all_to_all(
            product.reshape(n_pair, p_grp, width), "pair", 0, 0, tiled=True
        )
        blocks = [held]
        srcs = [virt_idx]
        for bit in bits:
            perm = [(v, v ^ bit) for v in range(n_virt)]
            got = [lax.ppermute(x, "virt", perm) for x in blocks]
            blocks = blocks + got
            srcs = srcs + [s ^ bit for s in srcs]
        allb = jnp.concatenate(blocks, axis=0)
        src_tiles = jnp.concatenate([jnp.take(tout, s, axis=1) for s in srcs])
        one_hot = (src_tiles[:, None] == my_tiles[None, :]).astype(jnp.bfloat16)
        pieces.append(
            jnp.einsum("rpo,rt->pto", allb, one_hot, preferred_element_type=jnp.float32)
        )
    ladder = jnp.concatenate(pieces, axis=2) if N_CHUNK > 1 else pieces[0]
    return (ladder + onebody).astype(jnp.bfloat16)


def solution(mesh):
    return jax.shard_map(
        per_device,
        mesh=mesh,
        in_specs=(P(("pair", "virt"), None, None), P(("pair", "virt"), None, None), P(), P(), P()),
        out_specs=P("pair", "virt", None),
        check_vma=False,
    )
```

```python
import jax
import jax.numpy as jnp
from jax import lax
from jax.sharding import PartitionSpec as P

TILE = 64
NVT = 8
AS = 32
N_CHUNK = 1


def per_device(amps_pm, integrals, fock_vv, blk_tiles, blk_mask):
    n_virt = lax.axis_size("virt")
    n_pair = lax.axis_size("pair")
    n_dev = n_virt * n_pair
    pm_rows, n_tiles, tile_len = amps_pm.shape
    out_cols = integrals.shape[2]
    slab = n_tiles // n_virt
    device = lax.axis_index(("pair", "virt"))
    virt_idx = lax.axis_index("virt")
    p_grp = pm_rows * n_virt

    tin_all = blk_tiles[:, 0]
    tile_ids = jnp.arange(n_tiles, dtype=jnp.int32)
    pick = (tin_all[:, None] == tile_ids[None, :]).astype(amps_pm.dtype)
    picked = jnp.einsum(
        "dt,itc->dic", pick, amps_pm, preferred_element_type=jnp.float32
    ).astype(amps_pm.dtype)
    chosen = lax.all_to_all(picked, ("pair", "virt"), 0, 0, tiled=True)
    chosen = chosen.reshape(n_dev * pm_rows, tile_len)

    got = [lax.dynamic_slice_in_dim(amps_pm[:, :, :out_cols], virt_idx * slab, slab, 1)]
    for k in range(1, n_virt):
        part = lax.dynamic_slice_in_dim(
            amps_pm[:, :, :out_cols], ((virt_idx + k) % n_virt) * slab, slab, 1
        )
        perm = [(u, (u + k) % n_virt) for u in range(n_virt)]
        got.append(lax.ppermute(part, "virt", perm))
    stacked = jnp.stack(got)
    order = (virt_idx - jnp.arange(n_virt, dtype=jnp.int32)) % n_virt
    sub = jnp.take(stacked, order, axis=0)
    sub = sub.reshape(p_grp, slab // NVT, NVT, AS, TILE)
    fock_four = fock_vv.reshape(NVT, TILE, NVT, TILE)
    onebody = jnp.einsum(
        "pkqsd,bjqd->pkbsj", sub, fock_four, preferred_element_type=jnp.float32
    ).reshape(p_grp, slab, out_cols)

    own_mask = lax.dynamic_index_in_dim(blk_mask, device, 0, keepdims=False)
    own_mask = own_mask.astype(jnp.float32)

    tout = blk_tiles[:, 1].reshape(n_pair, n_virt)
    my_tiles = virt_idx * slab + jnp.arange(slab, dtype=jnp.int32)
    bits = []
    b = n_virt // 2
    while b >= 1:
        bits.append(b)
        b //= 2

    width = out_cols // N_CHUNK
    pieces = []
    for c in range(N_CHUNK):
        cols = integrals[0, :, c * width:(c + 1) * width]
        product = jnp.dot(chosen, cols, preferred_element_type=jnp.float32)
        product = (product * own_mask).astype(jnp.bfloat16)
        held = lax.all_to_all(
            product.reshape(n_pair, p_grp, width), "pair", 0, 0, tiled=True
        )
        blocks = [held]
        srcs = [virt_idx]
        for bit in bits:
            perm = [(v, v ^ bit) for v in range(n_virt)]
            got = [lax.ppermute(x, "virt", perm) for x in blocks]
            blocks = blocks + got
            srcs = srcs + [s ^ bit for s in srcs]
        allb = jnp.concatenate(blocks, axis=0)
        src_tiles = jnp.concatenate([jnp.take(tout, s, axis=1) for s in srcs])
        one_hot = (src_tiles[:, None] == my_tiles[None, :]).astype(jnp.bfloat16)
        pieces.append(
            jnp.einsum("rpo,rt->pto", allb, one_hot, preferred_element_type=jnp.float32)
        )
    ladder = jnp.concatenate(pieces, axis=2) if N_CHUNK > 1 else pieces[0]
    return (ladder + onebody).astype(jnp.bfloat16)


def solution(mesh):
    return jax.shard_map(
        per_device,
        mesh=mesh,
        in_specs=(P(("pair", "virt"), None, None), P(("pair", "virt"), None, None), P(), P(), P()),
        out_specs=P("pair", "virt", None),
        check_vma=False,
    )
```

```python
import jax
import jax.numpy as jnp
from jax import lax
from jax.experimental import pallas as pl
from jax.experimental.pallas import tpu as pltpu
from jax.sharding import PartitionSpec as P

TILE = 64
NVT = 8
AS = 32
N_CHUNK = 1
TK = 512


def _ladder_kernel(mask_ref, a_ref, w_ref, o_ref, acc_ref):
    k = pl.program_id(0)

    @pl.when(k == 0)
    def _():
        acc_ref[...] = jnp.zeros_like(acc_ref)

    start = pl.multiple_of(k * TK, TK)
    acc_ref[...] += jnp.dot(
        a_ref[:, pl.ds(start, TK)], w_ref[0], preferred_element_type=jnp.float32
    )

    @pl.when(k == pl.num_programs(0) - 1)
    def _():
        scale = mask_ref[0].astype(jnp.float32)
        o_ref[...] = (acc_ref[...] * scale).astype(o_ref.dtype)


def ladder_matmul(mask, a, w):
    m, kdim = a.shape
    n = w.shape[2]
    return pl.pallas_call(
        _ladder_kernel,
        out_shape=jax.ShapeDtypeStruct((m, n), jnp.bfloat16),
        grid_spec=pltpu.PrefetchScalarGridSpec(
            num_scalar_prefetch=1,
            grid=(kdim // TK,),
            in_specs=[
                pl.BlockSpec((m, kdim), lambda k, s: (0, 0)),
                pl.BlockSpec((1, TK, n), lambda k, s: (0, k, 0)),
            ],
            out_specs=pl.BlockSpec((m, n), lambda k, s: (0, 0)),
            scratch_shapes=[pltpu.VMEM((m, n), jnp.float32)],
        ),
        compiler_params=pltpu.CompilerParams(dimension_semantics=("arbitrary",)),
        cost_estimate=pl.CostEstimate(
            flops=2 * m * kdim * n,
            transcendentals=0,
            bytes_accessed=kdim * n * 2 + m * kdim * 2 + m * n * 2,
        ),
    )(mask, a, w)


def per_device(amps_pm, integrals, fock_vv, blk_tiles, blk_mask):
    n_virt = lax.axis_size("virt")
    n_pair = lax.axis_size("pair")
    n_dev = n_virt * n_pair
    pm_rows, n_tiles, tile_len = amps_pm.shape
    out_cols = integrals.shape[2]
    slab = n_tiles // n_virt
    device = lax.axis_index(("pair", "virt"))
    virt_idx = lax.axis_index("virt")
    p_grp = pm_rows * n_virt

    tin_all = blk_tiles[:, 0]
    tile_ids = jnp.arange(n_tiles, dtype=jnp.int32)
    pick = (tin_all[:, None] == tile_ids[None, :]).astype(amps_pm.dtype)
    picked = jnp.einsum(
        "dt,itc->dic", pick, amps_pm, preferred_element_type=jnp.float32
    ).astype(amps_pm.dtype)
    chosen = lax.all_to_all(picked, ("pair", "virt"), 0, 0, tiled=True)
    chosen = chosen.reshape(n_dev * pm_rows, tile_len)

    got = [lax.dynamic_slice_in_dim(amps_pm[:, :, :out_cols], virt_idx * slab, slab, 1)]
    for k in range(1, n_virt):
        part = lax.dynamic_slice_in_dim(
            amps_pm[:, :, :out_cols], ((virt_idx + k) % n_virt) * slab, slab, 1
        )
        perm = [(u, (u + k) % n_virt) for u in range(n_virt)]
        got.append(lax.ppermute(part, "virt", perm))
    stacked = jnp.stack(got)
    order = (virt_idx - jnp.arange(n_virt, dtype=jnp.int32)) % n_virt
    reorder = (order[:, None] == jnp.arange(n_virt, dtype=jnp.int32)[None, :])
    sub = jnp.einsum(
        "uk,kptc->uptc", reorder.astype(stacked.dtype), stacked,
        preferred_element_type=jnp.float32,
    ).astype(stacked.dtype)
    sub = sub.reshape(p_grp, slab // NVT, NVT, AS, TILE)
    fock_four = fock_vv.reshape(NVT, TILE, NVT, TILE)
    onebody = jnp.einsum(
        "pkqsd,bjqd->pkbsj", sub, fock_four, preferred_element_type=jnp.float32
    ).reshape(p_grp, slab, out_cols)

    own_mask = lax.dynamic_slice_in_dim(blk_mask, device, 1, 0)

    tout = blk_tiles[:, 1].reshape(n_pair, n_virt)
    my_tiles = virt_idx * slab + jnp.arange(slab, dtype=jnp.int32)
    bits = []
    b = n_virt // 2
    while b >= 1:
        bits.append(b)
        b //= 2

    width = out_cols // N_CHUNK
    pieces = []
    for c in range(N_CHUNK):
        cols = integrals[:, :, c * width:(c + 1) * width]
        product = ladder_matmul(own_mask, chosen, cols)
        held = lax.all_to_all(
            product.reshape(n_pair, p_grp, width), "pair", 0, 0, tiled=True
        )
        blocks = [held]
        srcs = [virt_idx]
        for bit in bits:
            perm = [(v, v ^ bit) for v in range(n_virt)]
            got = [lax.ppermute(x, "virt", perm) for x in blocks]
            blocks = blocks + got
            srcs = srcs + [s ^ bit for s in srcs]
        allb = jnp.concatenate(blocks, axis=0)
        src_tiles = jnp.concatenate([jnp.take(tout, s, axis=1) for s in srcs])
        one_hot = (src_tiles[:, None] == my_tiles[None, :]).astype(jnp.bfloat16)
        pieces.append(
            jnp.einsum("rpo,rt->pto", allb, one_hot, preferred_element_type=jnp.float32)
        )
    ladder = jnp.concatenate(pieces, axis=2) if N_CHUNK > 1 else pieces[0]
    return (ladder + onebody).astype(jnp.bfloat16)


def solution(mesh):
    return jax.shard_map(
        per_device,
        mesh=mesh,
        in_specs=(P(("pair", "virt"), None, None), P(("pair", "virt"), None, None), P(), P(), P()),
        out_specs=P("pair", "virt", None),
        check_vma=False,
    )
```

```python
import jax
import jax.numpy as jnp
from jax import lax
from jax.experimental import pallas as pl
from jax.experimental.pallas import tpu as pltpu
from jax.sharding import PartitionSpec as P

TILE = 64
NVT = 8
AS = 32
N_CHUNK = 1
TK = 512


def _ladder_kernel(mask_ref, a_ref, w_ref, o_ref, acc_ref):
    k = pl.program_id(0)

    @pl.when(k == 0)
    def _():
        acc_ref[...] = jnp.zeros_like(acc_ref)

    start = pl.multiple_of(k * TK, TK)
    acc_ref[...] += jnp.dot(
        a_ref[:, pl.ds(start, TK)], w_ref[0], preferred_element_type=jnp.float32
    )

    @pl.when(k == pl.num_programs(0) - 1)
    def _():
        scale = mask_ref[0].astype(jnp.float32)
        o_ref[...] = (acc_ref[...] * scale).astype(o_ref.dtype)


def ladder_matmul(mask, a, w):
    m, kdim = a.shape
    n = w.shape[2]
    return pl.pallas_call(
        _ladder_kernel,
        out_shape=jax.ShapeDtypeStruct((m, n), jnp.bfloat16),
        grid_spec=pltpu.PrefetchScalarGridSpec(
            num_scalar_prefetch=1,
            grid=(kdim // TK,),
            in_specs=[
                pl.BlockSpec((m, kdim), lambda k, s: (0, 0)),
                pl.BlockSpec((1, TK, n), lambda k, s: (0, k, 0)),
            ],
            out_specs=pl.BlockSpec((m, n), lambda k, s: (0, 0)),
            scratch_shapes=[pltpu.VMEM((m, n), jnp.float32)],
        ),
        compiler_params=pltpu.CompilerParams(dimension_semantics=("arbitrary",)),
        cost_estimate=pl.CostEstimate(
            flops=2 * m * kdim * n,
            transcendentals=0,
            bytes_accessed=kdim * n * 2 + m * kdim * 2 + m * n * 2,
        ),
    )(mask, a, w)


def per_device(amps_pm, integrals, fock_vv, blk_tiles, blk_mask):
    n_virt = lax.axis_size("virt")
    n_pair = lax.axis_size("pair")
    n_dev = n_virt * n_pair
    pm_rows, n_tiles, tile_len = amps_pm.shape
    out_cols = integrals.shape[2]
    slab = n_tiles // n_virt
    device = lax.axis_index(("pair", "virt"))
    virt_idx = lax.axis_index("virt")
    pair_idx = lax.axis_index("pair")
    p_grp = pm_rows * n_virt

    tin_all = blk_tiles[:, 0]
    tile_ids = jnp.arange(n_tiles, dtype=jnp.int32)
    pick = (tin_all[:, None] == tile_ids[None, :]).astype(amps_pm.dtype)
    picked = jnp.einsum(
        "dt,itc->dic", pick, amps_pm, preferred_element_type=jnp.float32
    ).astype(amps_pm.dtype)
    chosen = lax.all_to_all(picked, ("pair", "virt"), 0, 0, tiled=True)
    chosen = chosen.reshape(n_dev * pm_rows, tile_len)

    got = [lax.dynamic_slice_in_dim(amps_pm[:, :, :out_cols], virt_idx * slab, slab, 1)]
    for k in range(1, n_virt):
        part = lax.dynamic_slice_in_dim(
            amps_pm[:, :, :out_cols], ((virt_idx + k) % n_virt) * slab, slab, 1
        )
        perm = [(u, (u + k) % n_virt) for u in range(n_virt)]
        got.append(lax.ppermute(part, "virt", perm))
    stacked = jnp.stack(got)
    order = (virt_idx - jnp.arange(n_virt, dtype=jnp.int32)) % n_virt
    reorder = (order[:, None] == jnp.arange(n_virt, dtype=jnp.int32)[None, :])
    sub = jnp.einsum(
        "uk,kptc->uptc", reorder.astype(stacked.dtype), stacked,
        preferred_element_type=jnp.float32,
    ).astype(stacked.dtype)
    sub = sub.reshape(p_grp, slab // NVT, NVT, AS, TILE)
    fock_four = fock_vv.reshape(NVT, TILE, NVT, TILE)
    onebody = jnp.einsum(
        "pkqsd,bjqd->pkbsj", sub, fock_four, preferred_element_type=jnp.float32
    ).reshape(p_grp, slab, out_cols)

    own_mask = lax.dynamic_slice_in_dim(blk_mask, device, 1, 0)

    tout = blk_tiles[:, 1].reshape(n_pair, n_virt)
    my_tiles = virt_idx * slab + jnp.arange(slab, dtype=jnp.int32)
    bits = []
    b = n_virt // 2
    while b >= 1:
        bits.append(b)
        b //= 2

    width = out_cols // N_CHUNK
    pieces = []
    for c in range(N_CHUNK):
        cols = integrals[0, :, c * width:(c + 1) * width]
        product = jnp.dot(chosen, cols, preferred_element_type=jnp.float32)
        product = (product * own_mask.astype(jnp.float32)).astype(jnp.bfloat16)
        product = product.reshape(n_pair, p_grp, width)
        pieces_a = [lax.dynamic_index_in_dim(product, pair_idx, 0)]
        src_pair = [pair_idx]
        for k in range(1, n_pair):
            part = lax.dynamic_index_in_dim(product, (pair_idx + k) % n_pair, 0)
            perm = [(g, (g + k) % n_pair) for g in range(n_pair)]
            pieces_a.append(lax.ppermute(part, "pair", perm))
            src_pair.append((pair_idx - k) % n_pair)
        held = jnp.concatenate(pieces_a, axis=0)
        src_pair = jnp.stack(src_pair)
        blocks = [held]
        srcs = [virt_idx]
        for bit in bits:
            perm = [(v, v ^ bit) for v in range(n_virt)]
            got = [lax.ppermute(x, "virt", perm) for x in blocks]
            blocks = blocks + got
            srcs = srcs + [s ^ bit for s in srcs]
        allb = jnp.concatenate(blocks, axis=0)
        src_tiles = jnp.concatenate([tout[src_pair, s] for s in srcs])
        one_hot = (src_tiles[:, None] == my_tiles[None, :]).astype(jnp.bfloat16)
        pieces.append(
            jnp.einsum("rpo,rt->pto", allb, one_hot, preferred_element_type=jnp.float32)
        )
    ladder = jnp.concatenate(pieces, axis=2) if N_CHUNK > 1 else pieces[0]
    return (ladder + onebody).astype(jnp.bfloat16)


def solution(mesh):
    return jax.shard_map(
        per_device,
        mesh=mesh,
        in_specs=(P(("pair", "virt"), None, None), P(("pair", "virt"), None, None), P(), P(), P()),
        out_specs=P("pair", "virt", None),
        check_vma=False,
    )
```

```python
import jax
import jax.numpy as jnp
from jax import lax
from jax.sharding import PartitionSpec as P

TILE = 64
NVT = 8
AS = 32
N_CHUNK = 1


def per_device(amps_pm, integrals, fock_vv, blk_tiles, blk_mask):
    n_virt = lax.axis_size("virt")
    n_pair = lax.axis_size("pair")
    n_dev = n_virt * n_pair
    pm_rows, n_tiles, tile_len = amps_pm.shape
    out_cols = integrals.shape[2]
    slab = n_tiles // n_virt
    device = lax.axis_index(("pair", "virt"))
    virt_idx = lax.axis_index("virt")
    p_grp = pm_rows * n_virt

    tin_all = blk_tiles[:, 0]
    tile_ids = jnp.arange(n_tiles, dtype=jnp.int32)
    pick = (tin_all[:, None] == tile_ids[None, :]).astype(amps_pm.dtype)
    picked = jnp.einsum(
        "dt,itc->dic", pick, amps_pm, preferred_element_type=jnp.float32
    ).astype(amps_pm.dtype)
    chosen = lax.all_to_all(picked, ("pair", "virt"), 0, 0, tiled=True)
    chosen = chosen.reshape(n_dev * pm_rows, tile_len)

    got = [lax.dynamic_slice_in_dim(amps_pm[:, :, :out_cols], virt_idx * slab, slab, 1)]
    for k in range(1, n_virt):
        part = lax.dynamic_slice_in_dim(
            amps_pm[:, :, :out_cols], ((virt_idx + k) % n_virt) * slab, slab, 1
        )
        perm = [(u, (u + k) % n_virt) for u in range(n_virt)]
        got.append(lax.ppermute(part, "virt", perm))
    stacked = jnp.stack(got)
    order = (virt_idx - jnp.arange(n_virt, dtype=jnp.int32)) % n_virt
    reorder = (order[:, None] == jnp.arange(n_virt, dtype=jnp.int32)[None, :])
    sub = jnp.einsum(
        "uk,kptc->uptc", reorder.astype(stacked.dtype), stacked,
        preferred_element_type=jnp.float32,
    ).astype(stacked.dtype)
    sub = sub.reshape(p_grp, slab // NVT, NVT, AS, TILE)
    fock_four = fock_vv.reshape(NVT, TILE, NVT, TILE)
    onebody = jnp.einsum(
        "pkqsd,bjqd->pkbsj", sub, fock_four, preferred_element_type=jnp.float32
    ).reshape(p_grp, slab, out_cols)

    chosen, onebody = lax.optimization_barrier((chosen, onebody))

    own_mask = lax.dynamic_index_in_dim(blk_mask, device, 0, keepdims=False)
    own_mask = own_mask.astype(jnp.float32)

    tout = blk_tiles[:, 1].reshape(n_pair, n_virt)
    my_tiles = virt_idx * slab + jnp.arange(slab, dtype=jnp.int32)
    bits = []
    b = n_virt // 2
    while b >= 1:
        bits.append(b)
        b //= 2

    width = out_cols // N_CHUNK
    pieces = []
    for c in range(N_CHUNK):
        cols = integrals[0, :, c * width:(c + 1) * width]
        product = jnp.dot(chosen, cols, preferred_element_type=jnp.float32)
        product = (product * own_mask).astype(jnp.bfloat16)
        held = lax.all_to_all(
            product.reshape(n_pair, p_grp, width), "pair", 0, 0, tiled=True
        )
        blocks = [held]
        srcs = [virt_idx]
        for bit in bits:
            perm = [(v, v ^ bit) for v in range(n_virt)]
            got = [lax.ppermute(x, "virt", perm) for x in blocks]
            blocks = blocks + got
            srcs = srcs + [s ^ bit for s in srcs]
        allb = jnp.concatenate(blocks, axis=0)
        src_tiles = jnp.concatenate([jnp.take(tout, s, axis=1) for s in srcs])
        one_hot = (src_tiles[:, None] == my_tiles[None, :]).astype(jnp.bfloat16)
        pieces.append(
            jnp.einsum("rpo,rt->pto", allb, one_hot, preferred_element_type=jnp.float32)
        )
    ladder = jnp.concatenate(pieces, axis=2) if N_CHUNK > 1 else pieces[0]
    return (ladder + onebody).astype(jnp.bfloat16)


def solution(mesh):
    return jax.shard_map(
        per_device,
        mesh=mesh,
        in_specs=(P(("pair", "virt"), None, None), P(("pair", "virt"), None, None), P(), P(), P()),
        out_specs=P("pair", "virt", None),
        check_vma=False,
    )
```

```python
import jax
import jax.numpy as jnp
from jax import lax
from jax.sharding import PartitionSpec as P

TILE = 64
NVT = 8
AS = 32
N_CHUNK = 1


def per_device(amps_pm, integrals, fock_vv, blk_tiles, blk_mask):
    n_virt = lax.axis_size("virt")
    n_pair = lax.axis_size("pair")
    n_dev = n_virt * n_pair
    pm_rows, n_tiles, tile_len = amps_pm.shape
    out_cols = integrals.shape[2]
    slab = n_tiles // n_virt
    device = lax.axis_index(("pair", "virt"))
    virt_idx = lax.axis_index("virt")
    p_grp = pm_rows * n_virt

    tin_all = blk_tiles[:, 0]
    tile_ids = jnp.arange(n_tiles, dtype=jnp.int32)
    pick = (tin_all[:, None] == tile_ids[None, :]).astype(amps_pm.dtype)
    picked = jnp.einsum(
        "dt,itc->dic", pick, amps_pm, preferred_element_type=jnp.float32
    ).astype(amps_pm.dtype)
    picked = picked.reshape(n_dev, pm_rows * tile_len)
    chosen = lax.all_to_all(picked, ("pair", "virt"), 0, 0, tiled=True)
    chosen = chosen.reshape(n_dev * pm_rows, tile_len)

    got = [lax.dynamic_slice_in_dim(amps_pm[:, :, :out_cols], virt_idx * slab, slab, 1)]
    for k in range(1, n_virt):
        part = lax.dynamic_slice_in_dim(
            amps_pm[:, :, :out_cols], ((virt_idx + k) % n_virt) * slab, slab, 1
        )
        perm = [(u, (u + k) % n_virt) for u in range(n_virt)]
        got.append(lax.ppermute(part, "virt", perm))
    stacked = jnp.stack(got)
    order = (virt_idx - jnp.arange(n_virt, dtype=jnp.int32)) % n_virt
    reorder = (order[:, None] == jnp.arange(n_virt, dtype=jnp.int32)[None, :])
    sub = jnp.einsum(
        "uk,kptc->uptc", reorder.astype(stacked.dtype), stacked,
        preferred_element_type=jnp.float32,
    ).astype(stacked.dtype)
    sub = sub.reshape(p_grp, slab // NVT, NVT, AS, TILE)
    fock_four = fock_vv.reshape(NVT, TILE, NVT, TILE)
    onebody = jnp.einsum(
        "pkqsd,bjqd->pkbsj", sub, fock_four, preferred_element_type=jnp.float32
    ).reshape(p_grp, slab, out_cols)

    own_mask = lax.dynamic_index_in_dim(blk_mask, device, 0, keepdims=False)
    own_mask = own_mask.astype(jnp.float32)

    tout = blk_tiles[:, 1].reshape(n_pair, n_virt)
    my_tiles = virt_idx * slab + jnp.arange(slab, dtype=jnp.int32)
    bits = []
    b = n_virt // 2
    while b >= 1:
        bits.append(b)
        b //= 2

    width = out_cols // N_CHUNK
    pieces = []
    for c in range(N_CHUNK):
        cols = integrals[0, :, c * width:(c + 1) * width]
        product = jnp.dot(chosen, cols, preferred_element_type=jnp.float32)
        product = (product * own_mask).astype(jnp.bfloat16)
        held = lax.all_to_all(
            product.reshape(n_pair, p_grp, width), "pair", 0, 0, tiled=True
        )
        blocks = [held]
        srcs = [virt_idx]
        for bit in bits:
            perm = [(v, v ^ bit) for v in range(n_virt)]
            got = lax.ppermute(jnp.concatenate(blocks, axis=0), "virt", perm)
            blocks = blocks + [got]
            srcs = srcs + [s ^ bit for s in srcs]
        allb = jnp.concatenate(blocks, axis=0)
        src_tiles = jnp.concatenate([jnp.take(tout, s, axis=1) for s in srcs])
        one_hot = (src_tiles[:, None] == my_tiles[None, :]).astype(jnp.bfloat16)
        pieces.append(
            jnp.einsum("rpo,rt->pto", allb, one_hot, preferred_element_type=jnp.float32)
        )
    ladder = jnp.concatenate(pieces, axis=2) if N_CHUNK > 1 else pieces[0]
    return (ladder + onebody).astype(jnp.bfloat16)


def solution(mesh):
    return jax.shard_map(
        per_device,
        mesh=mesh,
        in_specs=(P(("pair", "virt"), None, None), P(("pair", "virt"), None, None), P(), P(), P()),
        out_specs=P("pair", "virt", None),
        check_vma=False,
    )
```

```python
import jax
import jax.numpy as jnp
from jax import lax
from jax.sharding import PartitionSpec as P

TILE = 64
NVT = 8
AS = 32
N_CHUNK = 1


def per_device(amps_pm, integrals, fock_vv, blk_tiles, blk_mask):
    n_virt = lax.axis_size("virt")
    n_pair = lax.axis_size("pair")
    n_dev = n_virt * n_pair
    pm_rows, n_tiles, tile_len = amps_pm.shape
    out_cols = integrals.shape[2]
    slab = n_tiles // n_virt
    device = lax.axis_index(("pair", "virt"))
    virt_idx = lax.axis_index("virt")
    p_grp = pm_rows * n_virt

    tin_all = blk_tiles[:, 0]
    tile_ids = jnp.arange(n_tiles, dtype=jnp.int32)
    pick = (tin_all[:, None] == tile_ids[None, :]).astype(amps_pm.dtype)
    picked = jnp.einsum(
        "dt,itc->dic", pick, amps_pm, preferred_element_type=jnp.float32
    ).astype(amps_pm.dtype)
    chosen = lax.all_to_all(picked, ("pair", "virt"), 0, 0, tiled=True)
    chosen = chosen.reshape(n_dev * pm_rows, tile_len)

    got = [lax.dynamic_slice_in_dim(amps_pm[:, :, :out_cols], virt_idx * slab, slab, 1)]
    for k in range(1, n_virt):
        part = lax.dynamic_slice_in_dim(
            amps_pm[:, :, :out_cols], ((virt_idx + k) % n_virt) * slab, slab, 1
        )
        perm = [(u, (u + k) % n_virt) for u in range(n_virt)]
        got.append(lax.ppermute(part, "virt", perm))
    stacked = jnp.stack(got)
    order = (virt_idx - jnp.arange(n_virt, dtype=jnp.int32)) % n_virt
    reorder = (order[:, None] == jnp.arange(n_virt, dtype=jnp.int32)[None, :])
    sub = jnp.einsum(
        "uk,kptc->uptc", reorder.astype(stacked.dtype), stacked,
        preferred_element_type=jnp.float32,
    ).astype(stacked.dtype)
    sub = sub.reshape(p_grp, slab // NVT, NVT, AS, TILE)
    fock_four = fock_vv.reshape(NVT, TILE, NVT, TILE)
    onebody = jnp.einsum(
        "pkqsd,bjqd->pkbsj", sub, fock_four, preferred_element_type=jnp.float32
    ).reshape(p_grp, slab, out_cols)

    own_mask = lax.dynamic_index_in_dim(blk_mask, device, 0, keepdims=False)
    own_mask = own_mask.astype(jnp.float32)

    tout = blk_tiles[:, 1].reshape(n_pair, n_virt)
    my_tiles = virt_idx * slab + jnp.arange(slab, dtype=jnp.int32)
    bits = []
    b = n_virt // 2
    while b >= 1:
        bits.append(b)
        b //= 2

    width = out_cols // N_CHUNK
    pieces = []
    for c in range(N_CHUNK):
        cols = integrals[0, :, c * width:(c + 1) * width]
        product = jnp.dot(chosen, cols, preferred_element_type=jnp.float32)
        product = (product * own_mask).astype(jnp.bfloat16)
        held = lax.all_to_all(
            product.reshape(n_pair, p_grp, width), "pair", 0, 0, tiled=True
        )
        blocks = [held]
        srcs = [virt_idx]
        for bit in bits:
            perm = [(v, v ^ bit) for v in range(n_virt)]
            got = lax.ppermute(jnp.concatenate(blocks, axis=0), "virt", perm)
            blocks = blocks + [got]
            srcs = srcs + [s ^ bit for s in srcs]
        allb = jnp.concatenate(blocks, axis=0)
        src_tiles = jnp.concatenate([jnp.take(tout, s, axis=1) for s in srcs])
        one_hot = (src_tiles[:, None] == my_tiles[None, :]).astype(jnp.bfloat16)
        pieces.append(
            jnp.einsum("rpo,rt->pto", allb, one_hot, preferred_element_type=jnp.float32)
        )
    ladder = jnp.concatenate(pieces, axis=2) if N_CHUNK > 1 else pieces[0]
    return (ladder + onebody).astype(jnp.bfloat16)


def solution(mesh):
    return jax.shard_map(
        per_device,
        mesh=mesh,
        in_specs=(P(("pair", "virt"), None, None), P(("pair", "virt"), None, None), P(), P(), P()),
        out_specs=P("pair", "virt", None),
        check_vma=False,
    )
```

```python
import jax
import jax.numpy as jnp
from jax import lax
from jax.sharding import PartitionSpec as P

TILE = 64
NVT = 8
AS = 32
N_CHUNK = 1


def per_device(amps_pm, integrals, fock_vv, blk_tiles, blk_mask):
    n_virt = lax.axis_size("virt")
    n_pair = lax.axis_size("pair")
    n_dev = n_virt * n_pair
    pm_rows, n_tiles, tile_len = amps_pm.shape
    out_cols = integrals.shape[2]
    slab = n_tiles // n_virt
    device = lax.axis_index(("pair", "virt"))
    virt_idx = lax.axis_index("virt")
    p_grp = pm_rows * n_virt

    tin_all = blk_tiles[:, 0]
    tile_ids = jnp.arange(n_tiles, dtype=jnp.int32)
    pick = (tin_all[:, None] == tile_ids[None, :]).astype(amps_pm.dtype)
    picked = jnp.einsum(
        "dt,itc->dic", pick, amps_pm, preferred_element_type=jnp.float32
    ).astype(amps_pm.dtype)
    chosen = lax.all_to_all(picked, ("pair", "virt"), 0, 0, tiled=True)
    chosen = chosen.reshape(n_dev * pm_rows, tile_len)

    got = [lax.dynamic_slice_in_dim(amps_pm[:, :, :out_cols], virt_idx * slab, slab, 1)]
    for k in range(1, n_virt):
        part = lax.dynamic_slice_in_dim(
            amps_pm[:, :, :out_cols], ((virt_idx + k) % n_virt) * slab, slab, 1
        )
        perm = [(u, (u + k) % n_virt) for u in range(n_virt)]
        got.append(lax.ppermute(part, "virt", perm))
    stacked = jnp.stack(got)
    order = (virt_idx - jnp.arange(n_virt, dtype=jnp.int32)) % n_virt
    reorder = (order[:, None] == jnp.arange(n_virt, dtype=jnp.int32)[None, :])
    fock_four = fock_vv.reshape(NVT, TILE, NVT, TILE)

    def one_body(stacked):
        sub = jnp.einsum(
            "uk,kptc->uptc", reorder.astype(stacked.dtype), stacked,
            preferred_element_type=jnp.float32,
        ).astype(stacked.dtype)
        sub = sub.reshape(p_grp, slab // NVT, NVT, AS, TILE)
        return jnp.einsum(
            "pkqsd,bjqd->pkbsj", sub, fock_four, preferred_element_type=jnp.float32
        ).reshape(p_grp, slab, out_cols)

    own_mask = lax.dynamic_index_in_dim(blk_mask, device, 0, keepdims=False)
    own_mask = own_mask.astype(jnp.float32)

    tout = blk_tiles[:, 1].reshape(n_pair, n_virt)
    my_tiles = virt_idx * slab + jnp.arange(slab, dtype=jnp.int32)
    bits = []
    b = n_virt // 2
    while b >= 1:
        bits.append(b)
        b //= 2

    width = out_cols // N_CHUNK
    pieces = []
    for c in range(N_CHUNK):
        cols = integrals[0, :, c * width:(c + 1) * width]
        product = jnp.dot(chosen, cols, preferred_element_type=jnp.float32)
        product = (product * own_mask).astype(jnp.bfloat16)
        product, stacked = lax.optimization_barrier((product, stacked))
        held = lax.all_to_all(
            product.reshape(n_pair, p_grp, width), "pair", 0, 0, tiled=True
        )
        onebody = one_body(stacked)
        held, onebody = lax.optimization_barrier((held, onebody))
        blocks = [held]
        srcs = [virt_idx]
        for bit in bits:
            perm = [(v, v ^ bit) for v in range(n_virt)]
            got = [lax.ppermute(x, "virt", perm) for x in blocks]
            blocks = blocks + got
            srcs = srcs + [s ^ bit for s in srcs]
        allb = jnp.concatenate(blocks, axis=0)
        src_tiles = jnp.concatenate([jnp.take(tout, s, axis=1) for s in srcs])
        one_hot = (src_tiles[:, None] == my_tiles[None, :]).astype(jnp.bfloat16)
        pieces.append(
            jnp.einsum("rpo,rt->pto", allb, one_hot, preferred_element_type=jnp.float32)
        )
    ladder = jnp.concatenate(pieces, axis=2) if N_CHUNK > 1 else pieces[0]
    return (ladder + onebody).astype(jnp.bfloat16)


def solution(mesh):
    return jax.shard_map(
        per_device,
        mesh=mesh,
        in_specs=(P(("pair", "virt"), None, None), P(("pair", "virt"), None, None), P(), P(), P()),
        out_specs=P("pair", "virt", None),
        check_vma=False,
    )
```

```python
import jax
import jax.numpy as jnp
from jax import lax
from jax.sharding import PartitionSpec as P

TILE = 64
NVT = 8
AS = 32
N_CHUNK = 1


def per_device(amps_pm, integrals, fock_vv, blk_tiles, blk_mask):
    n_virt = lax.axis_size("virt")
    n_pair = lax.axis_size("pair")
    n_dev = n_virt * n_pair
    pm_rows, n_tiles, tile_len = amps_pm.shape
    out_cols = integrals.shape[2]
    slab = n_tiles // n_virt
    device = lax.axis_index(("pair", "virt"))
    virt_idx = lax.axis_index("virt")
    p_grp = pm_rows * n_virt

    tin_all = blk_tiles[:, 0]
    tile_ids = jnp.arange(n_tiles, dtype=jnp.int32)
    pick = (tin_all[:, None] == tile_ids[None, :]).astype(amps_pm.dtype)
    picked = jnp.einsum(
        "dt,itc->dic", pick, amps_pm, preferred_element_type=jnp.float32
    ).astype(amps_pm.dtype)
    chosen = lax.all_to_all(picked, ("pair", "virt"), 0, 0, tiled=True)
    chosen = chosen.reshape(n_dev * pm_rows, tile_len)

    chosen, ob_src = lax.optimization_barrier((chosen, amps_pm[:, :, :out_cols]))
    got = [lax.dynamic_slice_in_dim(ob_src, virt_idx * slab, slab, 1)]
    for k in range(1, n_virt):
        part = lax.dynamic_slice_in_dim(
            ob_src, ((virt_idx + k) % n_virt) * slab, slab, 1
        )
        perm = [(u, (u + k) % n_virt) for u in range(n_virt)]
        got.append(lax.ppermute(part, "virt", perm))
    stacked = jnp.stack(got)
    order = (virt_idx - jnp.arange(n_virt, dtype=jnp.int32)) % n_virt
    reorder = (order[:, None] == jnp.arange(n_virt, dtype=jnp.int32)[None, :])
    fock_four = fock_vv.reshape(NVT, TILE, NVT, TILE)

    def one_body(stacked):
        sub = jnp.einsum(
            "uk,kptc->uptc", reorder.astype(stacked.dtype), stacked,
            preferred_element_type=jnp.float32,
        ).astype(stacked.dtype)
        sub = sub.reshape(p_grp, slab // NVT, NVT, AS, TILE)
        return jnp.einsum(
            "pkqsd,bjqd->pkbsj", sub, fock_four, preferred_element_type=jnp.float32
        ).reshape(p_grp, slab, out_cols)

    own_mask = lax.dynamic_index_in_dim(blk_mask, device, 0, keepdims=False)
    own_mask = own_mask.astype(jnp.float32)

    tout = blk_tiles[:, 1].reshape(n_pair, n_virt)
    my_tiles = virt_idx * slab + jnp.arange(slab, dtype=jnp.int32)
    bits = []
    b = n_virt // 2
    while b >= 1:
        bits.append(b)
        b //= 2

    width = out_cols // N_CHUNK
    pieces = []
    for c in range(N_CHUNK):
        cols = integrals[0, :, c * width:(c + 1) * width]
        product = jnp.dot(chosen, cols, preferred_element_type=jnp.float32)
        product = (product * own_mask).astype(jnp.bfloat16)
        product, stacked = lax.optimization_barrier((product, stacked))
        held = lax.all_to_all(
            product.reshape(n_pair, p_grp, width), "pair", 0, 0, tiled=True
        )
        onebody = one_body(stacked)
        held, onebody = lax.optimization_barrier((held, onebody))
        blocks = [held]
        srcs = [virt_idx]
        for bit in bits:
            perm = [(v, v ^ bit) for v in range(n_virt)]
            got = [lax.ppermute(x, "virt", perm) for x in blocks]
            blocks = blocks + got
            srcs = srcs + [s ^ bit for s in srcs]
        allb = jnp.concatenate(blocks, axis=0)
        src_tiles = jnp.concatenate([jnp.take(tout, s, axis=1) for s in srcs])
        one_hot = (src_tiles[:, None] == my_tiles[None, :]).astype(jnp.bfloat16)
        pieces.append(
            jnp.einsum("rpo,rt->pto", allb, one_hot, preferred_element_type=jnp.float32)
        )
    ladder = jnp.concatenate(pieces, axis=2) if N_CHUNK > 1 else pieces[0]
    return (ladder + onebody).astype(jnp.bfloat16)


def solution(mesh):
    return jax.shard_map(
        per_device,
        mesh=mesh,
        in_specs=(P(("pair", "virt"), None, None), P(("pair", "virt"), None, None), P(), P(), P()),
        out_specs=P("pair", "virt", None),
        check_vma=False,
    )
```

```python
import jax
import jax.numpy as jnp
from jax import lax
from jax.sharding import PartitionSpec as P

TILE = 64
NVT = 8
AS = 32
N_CHUNK = 1
N_CORE = 2


def per_device(amps_pm, integrals, fock_vv, blk_tiles, blk_mask):
    n_virt = lax.axis_size("virt")
    n_pair = lax.axis_size("pair")
    n_dev = n_virt * n_pair
    pm_rows, n_tiles, tile_len = amps_pm.shape
    out_cols = integrals.shape[2]
    slab = n_tiles // n_virt
    device = lax.axis_index(("pair", "virt"))
    virt_idx = lax.axis_index("virt")
    p_grp = pm_rows * n_virt

    tin_all = blk_tiles[:, 0]
    tile_ids = jnp.arange(n_tiles, dtype=jnp.int32)
    pick = (tin_all[:, None] == tile_ids[None, :]).astype(amps_pm.dtype)
    picked = jnp.einsum(
        "dt,itc->dic", pick, amps_pm, preferred_element_type=jnp.float32
    ).astype(amps_pm.dtype)
    chosen = lax.all_to_all(picked, ("pair", "virt"), 0, 0, tiled=True)
    chosen = chosen.reshape(n_dev * pm_rows, tile_len)

    got = [lax.dynamic_slice_in_dim(amps_pm[:, :, :out_cols], virt_idx * slab, slab, 1)]
    for k in range(1, n_virt):
        part = lax.dynamic_slice_in_dim(
            amps_pm[:, :, :out_cols], ((virt_idx + k) % n_virt) * slab, slab, 1
        )
        perm = [(u, (u + k) % n_virt) for u in range(n_virt)]
        got.append(lax.ppermute(part, "virt", perm))
    stacked = jnp.stack(got)
    order = (virt_idx - jnp.arange(n_virt, dtype=jnp.int32)) % n_virt
    reorder = (order[:, None] == jnp.arange(n_virt, dtype=jnp.int32)[None, :])
    fock_four = fock_vv.reshape(NVT, TILE, NVT, TILE)

    def one_body(stacked):
        sub = jnp.einsum(
            "uk,kptc->uptc", reorder.astype(stacked.dtype), stacked,
            preferred_element_type=jnp.float32,
        ).astype(stacked.dtype)
        sub = sub.reshape(p_grp, slab // NVT, NVT, AS, TILE)
        return jnp.einsum(
            "pkqsd,bjqd->pkbsj", sub, fock_four, preferred_element_type=jnp.float32
        ).reshape(p_grp, slab, out_cols)

    own_mask = lax.dynamic_index_in_dim(blk_mask, device, 0, keepdims=False)
    own_tout = lax.dynamic_index_in_dim(blk_tiles[:, 1], device, 0, keepdims=False)
    own_mask = own_mask.astype(jnp.float32)

    tout = blk_tiles[:, 1].reshape(n_pair, n_virt)
    my_tiles = virt_idx * slab + jnp.arange(slab, dtype=jnp.int32)
    bits = []
    b = n_virt // 2
    while b >= 1:
        bits.append(b)
        b //= 2

    width = out_cols // N_CHUNK
    pieces = []
    for c in range(N_CHUNK):
        cols = integrals[0, :, c * width:(c + 1) * width]
        product = jnp.dot(chosen, cols, preferred_element_type=jnp.float32)
        product = (product * own_mask).astype(jnp.bfloat16)
        product, stacked = lax.optimization_barrier((product, stacked))
        n_x = n_virt // N_CORE
        dest_x = (own_tout // slab) // N_CORE
        sel = (jnp.arange(n_x, dtype=jnp.int32) == dest_x).astype(product.dtype)
        outgoing = product.reshape(n_pair, 1, p_grp, width) * sel[None, :, None, None]
        outgoing = outgoing.reshape(n_pair * n_x, p_grp, width)
        groups = [[d for d in range(n_dev) if d % N_CORE == c] for c in range(N_CORE)]
        held = lax.all_to_all(
            outgoing, ("pair", "virt"), 0, 0, tiled=True, axis_index_groups=groups
        )
        onebody = one_body(stacked)
        held, onebody = lax.optimization_barrier((held, onebody))
        perm = [(v, v ^ 1) for v in range(n_virt)]
        other = lax.ppermute(held, "virt", perm)
        allb = jnp.concatenate([held, other], axis=0)
        my_core = virt_idx % N_CORE
        members = jnp.arange(n_dev // N_CORE, dtype=jnp.int32) * N_CORE
        tout_all = blk_tiles[:, 1]
        src_tiles = jnp.concatenate(
            [tout_all[members + my_core], tout_all[members + (1 - my_core)]]
        )
        one_hot = (src_tiles[:, None] == my_tiles[None, :]).astype(jnp.bfloat16)
        pieces.append(
            jnp.einsum("rpo,rt->pto", allb, one_hot, preferred_element_type=jnp.float32)
        )
    ladder = jnp.concatenate(pieces, axis=2) if N_CHUNK > 1 else pieces[0]
    return (ladder + onebody).astype(jnp.bfloat16)


def solution(mesh):
    return jax.shard_map(
        per_device,
        mesh=mesh,
        in_specs=(P(("pair", "virt"), None, None), P(("pair", "virt"), None, None), P(), P(), P()),
        out_specs=P("pair", "virt", None),
        check_vma=False,
    )
```

```python
import jax
import jax.numpy as jnp
from jax import lax
from jax.sharding import PartitionSpec as P

TILE = 64
NVT = 8
AS = 32
N_CHUNK = 1


def per_device(amps_pm, integrals, fock_vv, blk_tiles, blk_mask):
    n_virt = lax.axis_size("virt")
    n_pair = lax.axis_size("pair")
    n_dev = n_virt * n_pair
    pm_rows, n_tiles, tile_len = amps_pm.shape
    out_cols = integrals.shape[2]
    slab = n_tiles // n_virt
    device = lax.axis_index(("pair", "virt"))
    virt_idx = lax.axis_index("virt")
    p_grp = pm_rows * n_virt

    slot = jnp.arange(n_dev, dtype=jnp.int32)
    tin_all = blk_tiles[(slot % n_pair) * n_virt + slot // n_pair, 0]
    tile_ids = jnp.arange(n_tiles, dtype=jnp.int32)
    pick = (tin_all[:, None] == tile_ids[None, :]).astype(amps_pm.dtype)
    picked = jnp.einsum(
        "dt,itc->dic", pick, amps_pm, preferred_element_type=jnp.float32
    ).astype(amps_pm.dtype)
    chosen = lax.all_to_all(picked, ("virt", "pair"), 0, 0, tiled=True)
    chosen = jnp.transpose(
        chosen.reshape(n_virt, n_pair, pm_rows, tile_len), (1, 0, 2, 3)
    ).reshape(n_dev * pm_rows, tile_len)

    got = [lax.dynamic_slice_in_dim(amps_pm[:, :, :out_cols], virt_idx * slab, slab, 1)]
    for k in range(1, n_virt):
        part = lax.dynamic_slice_in_dim(
            amps_pm[:, :, :out_cols], ((virt_idx + k) % n_virt) * slab, slab, 1
        )
        perm = [(u, (u + k) % n_virt) for u in range(n_virt)]
        got.append(lax.ppermute(part, "virt", perm))
    stacked = jnp.stack(got)
    order = (virt_idx - jnp.arange(n_virt, dtype=jnp.int32)) % n_virt
    reorder = (order[:, None] == jnp.arange(n_virt, dtype=jnp.int32)[None, :])
    fock_four = fock_vv.reshape(NVT, TILE, NVT, TILE)

    def one_body(stacked):
        sub = jnp.einsum(
            "uk,kptc->uptc", reorder.astype(stacked.dtype), stacked,
            preferred_element_type=jnp.float32,
        ).astype(stacked.dtype)
        sub = sub.reshape(p_grp, slab // NVT, NVT, AS, TILE)
        return jnp.einsum(
            "pkqsd,bjqd->pkbsj", sub, fock_four, preferred_element_type=jnp.float32
        ).reshape(p_grp, slab, out_cols)

    own_mask = lax.dynamic_index_in_dim(blk_mask, device, 0, keepdims=False)
    own_mask = own_mask.astype(jnp.float32)

    tout = blk_tiles[:, 1].reshape(n_pair, n_virt)
    my_tiles = virt_idx * slab + jnp.arange(slab, dtype=jnp.int32)
    bits = []
    b = n_virt // 2
    while b >= 1:
        bits.append(b)
        b //= 2

    width = out_cols // N_CHUNK
    pieces = []
    for c in range(N_CHUNK):
        cols = integrals[0, :, c * width:(c + 1) * width]
        product = jnp.dot(chosen, cols, preferred_element_type=jnp.float32)
        product = (product * own_mask).astype(jnp.bfloat16)
        product, stacked = lax.optimization_barrier((product, stacked))
        held = lax.all_to_all(
            product.reshape(n_pair, p_grp, width), "pair", 0, 0, tiled=True
        )
        onebody = one_body(stacked)
        held, onebody = lax.optimization_barrier((held, onebody))
        blocks = [held]
        srcs = [virt_idx]
        for bit in bits:
            perm = [(v, v ^ bit) for v in range(n_virt)]
            got = [lax.ppermute(x, "virt", perm) for x in blocks]
            blocks = blocks + got
            srcs = srcs + [s ^ bit for s in srcs]
        allb = jnp.concatenate(blocks, axis=0)
        src_tiles = jnp.concatenate([jnp.take(tout, s, axis=1) for s in srcs])
        one_hot = (src_tiles[:, None] == my_tiles[None, :]).astype(jnp.bfloat16)
        pieces.append(
            jnp.einsum("rpo,rt->pto", allb, one_hot, preferred_element_type=jnp.float32)
        )
    ladder = jnp.concatenate(pieces, axis=2) if N_CHUNK > 1 else pieces[0]
    return (ladder + onebody).astype(jnp.bfloat16)


def solution(mesh):
    return jax.shard_map(
        per_device,
        mesh=mesh,
        in_specs=(P(("pair", "virt"), None, None), P(("pair", "virt"), None, None), P(), P(), P()),
        out_specs=P("pair", "virt", None),
        check_vma=False,
    )
```

```python
import jax
import jax.numpy as jnp
from jax import lax
from jax.sharding import PartitionSpec as P

TILE = 64
NVT = 8
AS = 32
N_CHUNK = 1


def per_device(amps_pm, integrals, fock_vv, blk_tiles, blk_mask):
    n_virt = lax.axis_size("virt")
    n_pair = lax.axis_size("pair")
    n_dev = n_virt * n_pair
    pm_rows, n_tiles, tile_len = amps_pm.shape
    out_cols = integrals.shape[2]
    slab = n_tiles // n_virt
    device = lax.axis_index(("pair", "virt"))
    virt_idx = lax.axis_index("virt")
    p_grp = pm_rows * n_virt

    tile_ids = jnp.arange(n_tiles, dtype=jnp.int32)
    col_in = (jnp.arange(2, dtype=jnp.int32) == 0)[None, :, None]
    pick = jnp.any(
        (blk_tiles[:, :, None] == tile_ids[None, None, :]) & col_in, axis=1
    ).astype(amps_pm.dtype)
    picked = jnp.einsum(
        "dt,itc->dic", pick, amps_pm, preferred_element_type=jnp.float32
    ).astype(amps_pm.dtype)
    chosen = lax.all_to_all(picked, ("pair", "virt"), 0, 0, tiled=True)
    chosen = chosen.reshape(n_dev * pm_rows, tile_len)

    got = [lax.dynamic_slice_in_dim(amps_pm[:, :, :out_cols], virt_idx * slab, slab, 1)]
    for k in range(1, n_virt):
        part = lax.dynamic_slice_in_dim(
            amps_pm[:, :, :out_cols], ((virt_idx + k) % n_virt) * slab, slab, 1
        )
        perm = [(u, (u + k) % n_virt) for u in range(n_virt)]
        got.append(lax.ppermute(part, "virt", perm))
    stacked = jnp.stack(got)
    order = (virt_idx - jnp.arange(n_virt, dtype=jnp.int32)) % n_virt
    reorder = (order[:, None] == jnp.arange(n_virt, dtype=jnp.int32)[None, :])
    fock_four = fock_vv.reshape(NVT, TILE, NVT, TILE)

    def one_body(stacked):
        sub = jnp.einsum(
            "uk,kptc->uptc", reorder.astype(stacked.dtype), stacked,
            preferred_element_type=jnp.float32,
        ).astype(stacked.dtype)
        sub = sub.reshape(p_grp, slab // NVT, NVT, AS, TILE)
        return jnp.einsum(
            "pkqsd,bjqd->pkbsj", sub, fock_four, preferred_element_type=jnp.float32
        ).reshape(p_grp, slab, out_cols)

    own_mask = lax.dynamic_index_in_dim(blk_mask, device, 0, keepdims=False)
    own_mask = own_mask.astype(jnp.float32)

    tout = blk_tiles[:, 1].reshape(n_pair, n_virt)
    my_tiles = virt_idx * slab + jnp.arange(slab, dtype=jnp.int32)
    bits = []
    b = n_virt // 2
    while b >= 1:
        bits.append(b)
        b //= 2

    width = out_cols // N_CHUNK
    pieces = []
    for c in range(N_CHUNK):
        cols = integrals[0, :, c * width:(c + 1) * width]
        product = jnp.dot(chosen, cols, preferred_element_type=jnp.float32)
        product = (product * own_mask).astype(jnp.bfloat16)
        product, stacked = lax.optimization_barrier((product, stacked))
        held = lax.all_to_all(
            product.reshape(n_pair, p_grp, width), "pair", 0, 0, tiled=True
        )
        onebody = one_body(stacked)
        held, onebody = lax.optimization_barrier((held, onebody))
        blocks = [held]
        srcs = [virt_idx]
        for bit in bits:
            perm = [(v, v ^ bit) for v in range(n_virt)]
            got = [lax.ppermute(x, "virt", perm) for x in blocks]
            blocks = blocks + got
            srcs = srcs + [s ^ bit for s in srcs]
        allb = jnp.concatenate(blocks, axis=0)
        src_tiles = jnp.concatenate([jnp.take(tout, s, axis=1) for s in srcs])
        one_hot = (src_tiles[:, None] == my_tiles[None, :]).astype(jnp.bfloat16)
        pieces.append(
            jnp.einsum("rpo,rt->pto", allb, one_hot, preferred_element_type=jnp.float32)
        )
    ladder = jnp.concatenate(pieces, axis=2) if N_CHUNK > 1 else pieces[0]
    return (ladder + onebody).astype(jnp.bfloat16)


def solution(mesh):
    return jax.shard_map(
        per_device,
        mesh=mesh,
        in_specs=(P(("pair", "virt"), None, None), P(("pair", "virt"), None, None), P(), P(), P()),
        out_specs=P("pair", "virt", None),
        check_vma=False,
    )
```

```python
import jax
import jax.numpy as jnp
from jax import lax
from jax.sharding import PartitionSpec as P

TILE = 64
NVT = 8
AS = 32
N_CHUNK = 1


def per_device(amps_pm, integrals, fock_vv, blk_tiles, blk_mask):
    n_virt = lax.axis_size("virt")
    n_pair = lax.axis_size("pair")
    n_dev = n_virt * n_pair
    pm_rows, n_tiles, tile_len = amps_pm.shape
    out_cols = integrals.shape[2]
    slab = n_tiles // n_virt
    device = lax.axis_index(("pair", "virt"))
    virt_idx = lax.axis_index("virt")
    p_grp = pm_rows * n_virt

    tin_all = blk_tiles[:, 0]
    tile_ids = jnp.arange(n_tiles, dtype=jnp.int32)
    pick = (tin_all[:, None] == tile_ids[None, :]).astype(amps_pm.dtype)
    picked = jnp.einsum(
        "dt,itc->dic", pick, amps_pm, preferred_element_type=jnp.float32
    ).astype(amps_pm.dtype)
    chosen = lax.all_to_all(picked, ("pair", "virt"), 0, 0, tiled=True)
    chosen = chosen.reshape(n_dev * pm_rows, tile_len)

    got = [lax.dynamic_slice_in_dim(amps_pm[:, :, :out_cols], virt_idx * slab, slab, 1)]
    for k in range(1, n_virt):
        part = lax.dynamic_slice_in_dim(
            amps_pm[:, :, :out_cols], ((virt_idx + k) % n_virt) * slab, slab, 1
        )
        perm = [(u, (u + k) % n_virt) for u in range(n_virt)]
        got.append(lax.ppermute(part, "virt", perm))
    stacked = jnp.stack(got)
    order = (virt_idx - jnp.arange(n_virt, dtype=jnp.int32)) % n_virt
    reorder = (order[:, None] == jnp.arange(n_virt, dtype=jnp.int32)[None, :])
    fock_four = fock_vv.reshape(NVT, TILE, NVT, TILE)

    def one_body(stacked):
        sub = jnp.einsum(
            "uk,kptc->uptc", reorder.astype(stacked.dtype), stacked,
            preferred_element_type=jnp.float32,
        ).astype(stacked.dtype)
        sub = sub.reshape(p_grp, slab // NVT, NVT, AS, TILE)
        return jnp.einsum(
            "pkqsd,bjqd->pkbsj", sub, fock_four, preferred_element_type=jnp.float32
        ).reshape(p_grp, slab, out_cols)

    own_mask = lax.dynamic_index_in_dim(blk_mask, device, 0, keepdims=False)
    own_mask = own_mask.astype(jnp.float32)

    tout = blk_tiles[:, 1].reshape(n_pair, n_virt)
    my_tiles = virt_idx * slab + jnp.arange(slab, dtype=jnp.int32)
    bits = []
    b = n_virt // 2
    while b >= 1:
        bits.append(b)
        b //= 2

    width = out_cols // N_CHUNK
    pieces = []
    for c in range(N_CHUNK):
        cols = integrals[0, :, c * width:(c + 1) * width]
        product = jnp.dot(chosen, cols, preferred_element_type=jnp.float32)
        product = (product * own_mask).astype(jnp.bfloat16)
        product, stacked = lax.optimization_barrier((product, stacked))
        held = lax.all_to_all(
            product.reshape(n_pair, p_grp, width), "pair", 0, 0, tiled=True
        )
        onebody = one_body(stacked)
        held, onebody = lax.optimization_barrier((held, onebody))
        blocks = [held]
        srcs = [virt_idx]
        for bit in bits:
            perm = [(v, v ^ bit) for v in range(n_virt)]
            got = [lax.ppermute(x, "virt", perm) for x in blocks]
            blocks = blocks + got
            srcs = srcs + [s ^ bit for s in srcs]
        early = jnp.concatenate(blocks[:-1], axis=0)
        early_tiles = jnp.concatenate([jnp.take(tout, s, axis=1) for s in srcs[:-1]])
        one_hot = (early_tiles[:, None] == my_tiles[None, :]).astype(jnp.bfloat16)
        acc = onebody + jnp.einsum(
            "rpo,rt->pto", early, one_hot, preferred_element_type=jnp.float32
        )
        acc = lax.optimization_barrier(acc)
        late_hit = jnp.take(tout, srcs[-1], axis=1)[:, None] == my_tiles[None, :]
        late = blocks[-1].astype(jnp.float32)
        for r in range(late.shape[0]):
            acc = acc + jnp.where(late_hit[r][None, :, None], late[r][:, None, :], 0.0)
        pieces.append(acc)
    total = jnp.concatenate(pieces, axis=2) if N_CHUNK > 1 else pieces[0]
    return total.astype(jnp.bfloat16)


def solution(mesh):
    return jax.shard_map(
        per_device,
        mesh=mesh,
        in_specs=(P(("pair", "virt"), None, None), P(("pair", "virt"), None, None), P(), P(), P()),
        out_specs=P("pair", "virt", None),
        check_vma=False,
    )
```

```python
import jax
import jax.numpy as jnp
from jax import lax
from jax.sharding import PartitionSpec as P

TILE = 64
NVT = 8
AS = 32
N_CHUNK = 1


def per_device(amps_pm, integrals, fock_vv, blk_tiles, blk_mask):
    n_virt = lax.axis_size("virt")
    n_pair = lax.axis_size("pair")
    n_dev = n_virt * n_pair
    pm_rows, n_tiles, tile_len = amps_pm.shape
    out_cols = integrals.shape[2]
    slab = n_tiles // n_virt
    device = lax.axis_index(("pair", "virt"))
    virt_idx = lax.axis_index("virt")
    p_grp = pm_rows * n_virt

    tin_all = blk_tiles[:, 0]
    tile_ids = jnp.arange(n_tiles, dtype=jnp.int32)
    pick = (tin_all[:, None] == tile_ids[None, :]).astype(amps_pm.dtype)
    picked = jnp.einsum(
        "dt,itc->dic", pick, amps_pm, preferred_element_type=jnp.float32
    ).astype(amps_pm.dtype)
    half = tile_len // 2
    chosen = [
        lax.all_to_all(
            picked[:, :, h * half:(h + 1) * half], ("pair", "virt"), 0, 0, tiled=True
        ).reshape(n_dev * pm_rows, half)
        for h in range(2)
    ]

    got = [lax.dynamic_slice_in_dim(amps_pm[:, :, :out_cols], virt_idx * slab, slab, 1)]
    for k in range(1, n_virt):
        part = lax.dynamic_slice_in_dim(
            amps_pm[:, :, :out_cols], ((virt_idx + k) % n_virt) * slab, slab, 1
        )
        perm = [(u, (u + k) % n_virt) for u in range(n_virt)]
        got.append(lax.ppermute(part, "virt", perm))
    stacked = jnp.stack(got)
    order = (virt_idx - jnp.arange(n_virt, dtype=jnp.int32)) % n_virt
    reorder = (order[:, None] == jnp.arange(n_virt, dtype=jnp.int32)[None, :])
    fock_four = fock_vv.reshape(NVT, TILE, NVT, TILE)

    def one_body(stacked):
        sub = jnp.einsum(
            "uk,kptc->uptc", reorder.astype(stacked.dtype), stacked,
            preferred_element_type=jnp.float32,
        ).astype(stacked.dtype)
        sub = sub.reshape(p_grp, slab // NVT, NVT, AS, TILE)
        return jnp.einsum(
            "pkqsd,bjqd->pkbsj", sub, fock_four, preferred_element_type=jnp.float32
        ).reshape(p_grp, slab, out_cols)

    own_mask = lax.dynamic_index_in_dim(blk_mask, device, 0, keepdims=False)
    own_mask = own_mask.astype(jnp.float32)

    tout = blk_tiles[:, 1].reshape(n_pair, n_virt)
    my_tiles = virt_idx * slab + jnp.arange(slab, dtype=jnp.int32)
    bits = []
    b = n_virt // 2
    while b >= 1:
        bits.append(b)
        b //= 2

    width = out_cols // N_CHUNK
    pieces = []
    for c in range(N_CHUNK):
        cols = integrals[0, :, c * width:(c + 1) * width]
        product = jnp.dot(chosen[0], cols[:half], preferred_element_type=jnp.float32)
        product = product + jnp.dot(
            chosen[1], cols[half:], preferred_element_type=jnp.float32
        )
        product = (product * own_mask).astype(jnp.bfloat16)
        product, stacked = lax.optimization_barrier((product, stacked))
        held = lax.all_to_all(
            product.reshape(n_pair, p_grp, width), "pair", 0, 0, tiled=True
        )
        onebody = one_body(stacked)
        held, onebody = lax.optimization_barrier((held, onebody))
        blocks = [held]
        srcs = [virt_idx]
        for bit in bits:
            perm = [(v, v ^ bit) for v in range(n_virt)]
            got = [lax.ppermute(x, "virt", perm) for x in blocks]
            blocks = blocks + got
            srcs = srcs + [s ^ bit for s in srcs]
        allb = jnp.concatenate(blocks, axis=0)
        src_tiles = jnp.concatenate([jnp.take(tout, s, axis=1) for s in srcs])
        one_hot = (src_tiles[:, None] == my_tiles[None, :]).astype(jnp.bfloat16)
        pieces.append(
            jnp.einsum("rpo,rt->pto", allb, one_hot, preferred_element_type=jnp.float32)
        )
    ladder = jnp.concatenate(pieces, axis=2) if N_CHUNK > 1 else pieces[0]
    return (ladder + onebody).astype(jnp.bfloat16)


def solution(mesh):
    return jax.shard_map(
        per_device,
        mesh=mesh,
        in_specs=(P(("pair", "virt"), None, None), P(("pair", "virt"), None, None), P(), P(), P()),
        out_specs=P("pair", "virt", None),
        check_vma=False,
    )
```

```python
import jax
import jax.numpy as jnp
from jax import lax
from jax.sharding import PartitionSpec as P

TILE = 64
NVT = 8
AS = 32
N_CHUNK = 1


def per_device(amps_pm, integrals, fock_vv, blk_tiles, blk_mask):
    n_virt = lax.axis_size("virt")
    n_pair = lax.axis_size("pair")
    n_dev = n_virt * n_pair
    pm_rows, n_tiles, tile_len = amps_pm.shape
    out_cols = integrals.shape[2]
    slab = n_tiles // n_virt
    device = lax.axis_index(("pair", "virt"))
    virt_idx = lax.axis_index("virt")
    p_grp = pm_rows * n_virt

    tin_all = jnp.transpose(blk_tiles[:, 0].reshape(n_pair, n_virt)).reshape(-1)
    tile_ids = jnp.arange(n_tiles, dtype=jnp.int32)
    pick = (tin_all[:, None] == tile_ids[None, :]).astype(amps_pm.dtype)
    picked = jnp.einsum(
        "dt,itc->dic", pick, amps_pm, preferred_element_type=jnp.float32
    ).astype(amps_pm.dtype)
    picked = picked.reshape(n_virt, n_pair, pm_rows, tile_len)
    mid = lax.all_to_all(picked, "virt", 0, 0, tiled=True)
    mid = jnp.transpose(mid, (1, 0, 2, 3))
    chosen = lax.all_to_all(mid, "pair", 0, 0, tiled=True)
    chosen = chosen.reshape(n_dev * pm_rows, tile_len)

    got = [lax.dynamic_slice_in_dim(amps_pm[:, :, :out_cols], virt_idx * slab, slab, 1)]
    for k in range(1, n_virt):
        part = lax.dynamic_slice_in_dim(
            amps_pm[:, :, :out_cols], ((virt_idx + k) % n_virt) * slab, slab, 1
        )
        perm = [(u, (u + k) % n_virt) for u in range(n_virt)]
        got.append(lax.ppermute(part, "virt", perm))
    stacked = jnp.stack(got)
    order = (virt_idx - jnp.arange(n_virt, dtype=jnp.int32)) % n_virt
    reorder = (order[:, None] == jnp.arange(n_virt, dtype=jnp.int32)[None, :])
    fock_four = fock_vv.reshape(NVT, TILE, NVT, TILE)

    def one_body(stacked):
        sub = jnp.einsum(
            "uk,kptc->uptc", reorder.astype(stacked.dtype), stacked,
            preferred_element_type=jnp.float32,
        ).astype(stacked.dtype)
        sub = sub.reshape(p_grp, slab // NVT, NVT, AS, TILE)
        return jnp.einsum(
            "pkqsd,bjqd->pkbsj", sub, fock_four, preferred_element_type=jnp.float32
        ).reshape(p_grp, slab, out_cols)

    own_mask = lax.dynamic_index_in_dim(blk_mask, device, 0, keepdims=False)
    own_mask = own_mask.astype(jnp.float32)

    tout = blk_tiles[:, 1].reshape(n_pair, n_virt)
    my_tiles = virt_idx * slab + jnp.arange(slab, dtype=jnp.int32)
    bits = []
    b = n_virt // 2
    while b >= 1:
        bits.append(b)
        b //= 2

    width = out_cols // N_CHUNK
    pieces = []
    for c in range(N_CHUNK):
        cols = integrals[0, :, c * width:(c + 1) * width]
        product = jnp.dot(chosen, cols, preferred_element_type=jnp.float32)
        product = (product * own_mask).astype(jnp.bfloat16)
        product, stacked = lax.optimization_barrier((product, stacked))
        held = lax.all_to_all(
            product.reshape(n_pair, p_grp, width), "pair", 0, 0, tiled=True
        )
        onebody = one_body(stacked)
        held, onebody = lax.optimization_barrier((held, onebody))
        blocks = [held]
        srcs = [virt_idx]
        for bit in bits:
            perm = [(v, v ^ bit) for v in range(n_virt)]
            got = [lax.ppermute(x, "virt", perm) for x in blocks]
            blocks = blocks + got
            srcs = srcs + [s ^ bit for s in srcs]
        allb = jnp.concatenate(blocks, axis=0)
        src_tiles = jnp.concatenate([jnp.take(tout, s, axis=1) for s in srcs])
        one_hot = (src_tiles[:, None] == my_tiles[None, :]).astype(jnp.bfloat16)
        pieces.append(
            jnp.einsum("rpo,rt->pto", allb, one_hot, preferred_element_type=jnp.float32)
        )
    ladder = jnp.concatenate(pieces, axis=2) if N_CHUNK > 1 else pieces[0]
    return (ladder + onebody).astype(jnp.bfloat16)


def solution(mesh):
    return jax.shard_map(
        per_device,
        mesh=mesh,
        in_specs=(P(("pair", "virt"), None, None), P(("pair", "virt"), None, None), P(), P(), P()),
        out_specs=P("pair", "virt", None),
        check_vma=False,
    )
```
